256 devices in a mesh: blk: 64 (over z, x, core), head: 2 (over y_hi), dec: 2 (over y_lo).
Axes of the slice: x: 4, y: 4 (y_hi: 2, y_lo: 2; y = y_hi * 2 + y_lo), z: 8, core: 2. Of those that a mesh axis runs over, the one named last changes fastest.
Arguments:
- queries: bfloat16 [16384, 1536], P('blk', ('head', 'dec')), may hold values from -12 to 12
- key_vectors: bfloat16 [16384, 1536], P('blk', ('head', 'dec')), may hold values from -5 to 5
- values: bfloat16 [16384, 1536], P('blk', ('head', 'dec')), may hold values from -6 to 6
- lookback: int32 [12], replicated, may hold values from 0 to 5, as said below
- residual: bfloat16 [16384, 3072], P(('blk', 'head', 'dec')), may hold values from -0.1875 to 0.1875
- out_weight: bfloat16 [1536, 3072], P(('head', 'dec')), may hold values from -0.15625 to 0.15625
- branch_gate: float32 [3072], replicated, may hold values from 0.5 to 1.5
- final_shift: float32 [3072], replicated, may hold values from -0.5 to 0.5
- final_scale: float32 [3072], replicated, may hold values from -0.5 to 0.5
- final_weight: bfloat16 [3072, 64], replicated, may hold values from -0.109375 to 0.109375
- decoder_kernel: bfloat16 [432, 512], replicated, may hold values from -0.3125 to 0.3125
- decoder_bias: float32 [512], replicated, may hold values from -3 to 3
Outputs:
- features: bfloat16 [1024, 64, 512], P(('blk', 'head', 'dec'))
The draws below stay inside these ranges and needn't reach their ends.
Inputs may be any that keep to these rules, and one draw needn't show every extreme that they name: lookback[h] is how many frames before its own the queries of head h may see; some head sees 5 earlier frames and some head none.
All inputs are finite; a program needn't handle non-finite values.
Results may differ from the reference program's by a relative error of at most 0.02.
Values may be sent and summed in bfloat16 or wider, within the bound.
No kernel may reach another device: no remote copies, remote signals or barrier semaphores. Data moves between devices by JAX's collectives and lax.ppermute only.
A program may use at most 192 MiB of HBM per device.

```python
import jax
import jax.numpy as jnp
from jax import lax

HEADS = 12
DH = 128
D = 3072
LC = 16
CO = 512
FRAMES = 8
WINDOW = 5
PW = 32
SLAB = 256
HD = 1536
PC = 64
TOKENS = 16384


def anchor_pair(key):
    query_base = 3.0 * jax.random.normal(jax.random.fold_in(key, 11), (TOKENS, HD), jnp.float32)
    key_base = jax.random.normal(jax.random.fold_in(key, 12), (TOKENS, HD), jnp.float32)
    query_base = jnp.clip(query_base, -12.0, 12.0)
    key_base = jnp.clip(key_base, -5.0, 5.0)
    return (query_base, key_base)


def draw_queries(key, part):
    return anchor_pair(key)[0].astype(jnp.bfloat16)


def draw_key_vectors(key, part):
    return anchor_pair(key)[1].astype(jnp.bfloat16)


def draw_lookback(key, part):
    base = jax.random.randint(jax.random.fold_in(key, 21), (HEADS,), 0, WINDOW + 1, dtype=jnp.int32)
    widest_head = jax.random.randint(jax.random.fold_in(key, 22), (), 0, HEADS, dtype=jnp.int32)
    offset = jax.random.randint(jax.random.fold_in(key, 23), (), 1, HEADS, dtype=jnp.int32)
    narrow_head = (widest_head + offset) % HEADS
    head_ids = jnp.arange(HEADS, dtype=jnp.int32)
    base = jnp.where(head_ids == widest_head, WINDOW, base)
    base = jnp.where(head_ids == narrow_head, 0, base)
    return base.astype(jnp.int32)


def level_of(stream_key, extent, split, least, top_value):
    def one(position, shards_of):
        heights = jax.random.uniform(jax.random.fold_in(jax.random.fold_in(stream_key, 6), position), (shards_of,), jnp.float32, least / len(split), top_value / len(split))
        return jnp.repeat(jnp.exp(heights), extent[position] // shards_of).reshape((-1,) + (1,) * (len(extent) - position - 1))

    level = one(*split[0])
    for cut in split[1:]:
        level = level * one(*cut)
    return level


def centred(rng, extent, scale, bound, pieces=(), held_as=jnp.bfloat16):
    gain = level_of(rng, extent, pieces, -0.22, 0.18) if pieces else 1.0
    array = jax.random.normal(rng, extent, jnp.float32) * scale * gain
    return jnp.minimum(jnp.maximum(array, -bound), bound).astype(held_as)


def setup_inputs(seed: int = 0) -> dict:
    key_list = jax.random.split(jax.random.key(seed), 13)
    return {
        "queries": draw_queries(jax.random.fold_in(key_list[12], 71), 0),
        "key_vectors": draw_key_vectors(jax.random.fold_in(key_list[12], 71), 0),
        "values": centred(key_list[2], (TOKENS, HD), 1.0, 6.0, ((0, 64), (1, 4))),
        "lookback": draw_lookback(jax.random.fold_in(key_list[12], 71), 0),
        "residual": centred(key_list[4], (TOKENS, D), 0.03, 0.1875, ((0, 256),)),
        "out_weight": centred(key_list[5], (HD, D), HD ** -0.5, 0.15625, ((0, 4),)),
        "branch_gate": jnp.clip(jax.random.uniform(key_list[6], (D,), jnp.float32, 0.5, 1.5), 0.5, 1.5),
        "final_shift": jnp.clip(jax.random.uniform(key_list[7], (D,), jnp.float32, -0.5, 0.5), -0.5, 0.5),
        "final_scale": jnp.clip(jax.random.uniform(key_list[8], (D,), jnp.float32, -0.5, 0.5), -0.5, 0.5),
        "final_weight": centred(key_list[9], (D, PC), D ** -0.5, 0.109375),
        "decoder_kernel": centred(key_list[10], (27 * LC, CO), (27 * LC) ** -0.5, 0.3125),
        "decoder_bias": centred(key_list[11], (CO,), 0.5, 3.0, (), jnp.float32),
    }


def attend_head(query_head, key_head, value_head, lookback_head):
    frame_len = TOKENS // FRAMES
    key_frame = jnp.arange(TOKENS, dtype=jnp.int32) // frame_len
    query_blocks = query_head.reshape(TOKENS // SLAB, SLAB, DH)
    block_ids = jnp.arange(TOKENS // SLAB, dtype=jnp.int32)

    def one_block(inputs):
        block, block_id = inputs
        scores = jnp.dot(block, key_head.T, preferred_element_type=jnp.float32) * DH ** (-0.5)
        query_frame = (block_id * SLAB + jnp.arange(SLAB, dtype=jnp.int32)) // frame_len
        visible = (key_frame[None, :] <= query_frame[:, None]) & (key_frame[None, :] >= query_frame[:, None] - lookback_head)
        row_max = lax.optimization_barrier(jnp.max(jnp.where(visible, scores, -1e+30), axis=1))
        weights = jnp.where(visible, jnp.exp(scores - row_max[:, None]), 0.0).astype(jnp.bfloat16)
        row_total = lax.optimization_barrier(jnp.sum(weights.astype(jnp.float32), axis=1))
        mixed = jnp.dot(weights, value_head, preferred_element_type=jnp.float32)
        return mixed / row_total[:, None]
    return lax.map(one_block, (query_blocks, block_ids)).reshape(TOKENS, DH)

def reference(queries, key_vectors, values, lookback, residual, out_weight, branch_gate, final_shift, final_scale, final_weight, decoder_kernel, decoder_bias):
    query_heads = queries.reshape(TOKENS, HEADS, DH).transpose(1, 0, 2)
    key_heads = key_vectors.reshape(TOKENS, HEADS, DH).transpose(1, 0, 2)
    value_heads = values.reshape(TOKENS, HEADS, DH).transpose(1, 0, 2)

    def per_head(inputs):
        return attend_head(inputs[0], inputs[1], inputs[2], inputs[3])
    heads_out = lax.map(per_head, (query_heads, key_heads, value_heads, lookback))
    attended = heads_out.transpose(1, 0, 2).reshape(TOKENS, HD).astype(jnp.bfloat16)
    projected = jnp.dot(attended, out_weight, preferred_element_type=jnp.float32)
    hidden = residual.astype(jnp.float32) + branch_gate[None, :] * projected
    center = lax.optimization_barrier(jnp.mean(hidden, axis=1, keepdims=True))
    spread = lax.optimization_barrier(jnp.mean((hidden - center) ** 2, axis=1, keepdims=True))
    normed = ((hidden - center) * lax.rsqrt(spread + 1e-06) * (1.0 + final_scale[None, :]) + final_shift[None, :]).astype(jnp.bfloat16)
    patches = jnp.dot(normed, final_weight, preferred_element_type=jnp.float32).astype(jnp.bfloat16)
    frame_rows = TOKENS // (FRAMES * PW)
    height = 2 * frame_rows
    width = 2 * PW
    canvas = patches.reshape(FRAMES * frame_rows, PW, 2, 2, LC).transpose(0, 2, 1, 3, 4).reshape(FRAMES * height, width, LC)
    canvas = jnp.pad(canvas, ((1, 1), (0, 0), (0, 0)))
    framed = [canvas[g * height:g * height + height + 2] for g in range(FRAMES)]
    history = jnp.stack([framed[0], framed[0]] + framed)
    history = jnp.pad(history, ((0, 0), (0, 0), (1, 1), (0, 0)))
    summed = jnp.zeros((FRAMES * height * width, CO), jnp.float32)
    for time_tap in range(3):
        for row_tap in range(3):
            for column_tap in range(3):
                tap_index = (time_tap * 3 + row_tap) * 3 + column_tap
                window = history[time_tap:time_tap + FRAMES, row_tap:row_tap + height, column_tap:column_tap + width, :].reshape(-1, LC)
                summed = summed + jnp.dot(window, decoder_kernel[tap_index * LC:(tap_index + 1) * LC], preferred_element_type=jnp.float32)
    features = (summed + decoder_bias[None, :]).astype(jnp.bfloat16)
    return features.reshape(FRAMES * height, width, CO)
```

```python
import functools

import jax
import jax.numpy as jnp
from jax import lax
from jax.experimental import pallas as pl
from jax.experimental.pallas import tpu as pltpu
from jax.sharding import Mesh
from jax.sharding import PartitionSpec as P

DH = 128
LC = 16
FRAMES = 8
PW = 32

ROWS = ("z", "x", "core", "head", "dec")


def padded_2(cells, sides, width):
    for axis, dim in sides:
        count = lax.axis_size(axis)
        ends = count - 1
        head = lax.slice_in_dim(cells, 0, width, axis=dim)
        tail = lax.slice_in_dim(cells, cells.shape[dim] - width, cells.shape[dim], axis=dim)
        cells = jnp.concatenate(
            [
                lax.ppermute(tail, axis, [(i, (i + 1) % count) for i in range(ends)]),
                cells,
                lax.ppermute(head, axis, [((i + 1) % count, i) for i in range(ends)]),
            ],
            axis=dim,
        )
    return cells


def from_behind(x, axis, by):
    peers = lax.axis_size(axis)
    pairs = [(i, i + by) for i in range(peers) if 0 <= i + by < peers]
    return lax.ppermute(x, axis, pairs)


def attend_kernel(head_count, part_rows, sp_ref, q_ref, kv_ref, o_ref, m_sc, l_sc, acc_sc):
    step = pl.program_id(0)
    frame_now = sp_ref[0]
    first = sp_ref[1]
    frame = first + step
    hd = head_count * DH

    @pl.when(step == 0)
    def _():
        m_sc[...] = jnp.full(m_sc.shape, -1e30, jnp.float32)
        l_sc[...] = jnp.zeros(l_sc.shape, jnp.float32)
        acc_sc[...] = jnp.zeros(acc_sc.shape, jnp.float32)

    for h in range(head_count):
        seen = (frame <= frame_now) & (frame >= frame_now - sp_ref[2 + h])

        @pl.when(seen)
        def _():
            q = q_ref[:, h * DH:(h + 1) * DH]
            for c in range(kv_ref.shape[0]):
                k = kv_ref[c, :, h * DH:(h + 1) * DH]
                v = kv_ref[c, :, hd + h * DH:hd + (h + 1) * DH]
                s = lax.dot_general(
                    q, k, (((1,), (1,)), ((), ())), preferred_element_type=jnp.float32
                ) * DH ** (-0.5)
                m_old = m_sc[h]
                m_new = jnp.maximum(m_old, jnp.max(s, axis=1, keepdims=True))
                alpha = jnp.exp(m_old - m_new)
                p = jnp.exp(s - m_new).astype(jnp.bfloat16)
                l_sc[h] = alpha * l_sc[h] + jnp.sum(p.astype(jnp.float32), axis=1, keepdims=True)
                acc_sc[h] = alpha * acc_sc[h] + jnp.dot(p, v, preferred_element_type=jnp.float32)
                m_sc[h] = m_new

    @pl.when(step == pl.num_programs(0) - 1)
    def _():
        for h in range(head_count):
            o_ref[:, h * DH:(h + 1) * DH] = (acc_sc[h] / l_sc[h]).astype(o_ref.dtype)


def attend(scalars, queries, kv):
    parts, frames, part_rows, width = kv.shape
    rows, hd = queries.shape
    head_count = hd // DH

    def kv_map(step, sp):
        return (0, jnp.minimum(sp[1] + step, sp[0]), 0, 0)

    flops = 4 * rows * parts * part_rows * hd * 6
    return pl.pallas_call(
        functools.partial(attend_kernel, head_count, part_rows),
        out_shape=jax.ShapeDtypeStruct((rows, hd), jnp.bfloat16),
        grid_spec=pltpu.PrefetchScalarGridSpec(
            num_scalar_prefetch=1,
            grid=(frames,),
            in_specs=[
                pl.BlockSpec((rows, hd), lambda step, sp: (0, 0)),
                pl.BlockSpec((parts, None, part_rows, width), kv_map),
            ],
            out_specs=pl.BlockSpec((rows, hd), lambda step, sp: (0, 0)),
            scratch_shapes=[
                pltpu.VMEM((head_count, rows, 1), jnp.float32),
                pltpu.VMEM((head_count, rows, 1), jnp.float32),
                pltpu.VMEM((head_count, rows, DH), jnp.float32),
            ],
        ),
        compiler_params=pltpu.CompilerParams(
            dimension_semantics=("arbitrary",), vmem_limit_bytes=48 * 1024 * 1024
        ),
        cost_estimate=pl.CostEstimate(
            flops=flops,
            transcendentals=rows * parts * part_rows * head_count * 6,
            bytes_accessed=parts * part_rows * width * 2 * 6 + rows * hd * 4,
        ),
    )(scalars, queries, kv)


def per_device(
    queries,
    key_vectors,
    values,
    lookback,
    residual,
    out_weight,
    branch_gate,
    final_shift,
    final_scale,
    final_weight,
    decoder_kernel,
    decoder_bias,
):
    slab_rows = queries.shape[0]
    head_count = queries.shape[1] // DH
    frame_index = lax.axis_index("z")
    lookback_heads = lax.dynamic_slice_in_dim(
        lookback, lax.axis_index(("head", "dec")) * head_count, head_count
    )
    first_frame = jnp.maximum(frame_index - jnp.max(lookback_heads), 0)
    scalars = jnp.concatenate(
        [jnp.stack([frame_index, first_frame]).astype(jnp.int32), lookback_heads.astype(jnp.int32)]
    )

    kv = jnp.concatenate([key_vectors, values], axis=1)
    kv = lax.all_gather(kv, ("z", "x"), axis=0, tiled=True)
    kv = lax.all_gather(kv, "core", axis=0, tiled=False)
    parts = kv.shape[0]
    kv = kv.reshape(parts, FRAMES, kv.shape[1] // FRAMES, kv.shape[2])
    attended = attend(scalars, queries, kv)

    tokens_dev = slab_rows // lax.axis_size(("head", "dec"))
    projected = lax.psum_scatter(
        jnp.dot(attended, out_weight, preferred_element_type=jnp.float32).astype(jnp.bfloat16),
        ("head", "dec"),
        scatter_dimension=0,
        tiled=True,
    ).astype(jnp.float32)
    hidden = residual.astype(jnp.float32) + branch_gate[None, :] * projected
    center = jnp.mean(hidden, axis=1, keepdims=True)
    spread = jnp.mean((hidden - center) ** 2, axis=1, keepdims=True)
    normed = (
        (hidden - center) * lax.rsqrt(spread + 1e-06) * (1.0 + final_scale[None, :])
        + final_shift[None, :]
    ).astype(jnp.bfloat16)
    patches = jnp.dot(normed, final_weight, preferred_element_type=jnp.float32).astype(jnp.bfloat16)
    patch_rows = tokens_dev // PW
    tile_rows = 2 * patch_rows
    width = 2 * PW
    tile = (
        patches.reshape(patch_rows, PW, 2, 2, LC)
        .transpose(0, 2, 1, 3, 4)
        .reshape(tile_rows, width * LC)
    )
    padded = padded_2(tile, ((ROWS, 0),), 1)
    prior_one = from_behind(padded, "z", 1)
    prior_one = jnp.where(frame_index >= 1, prior_one, padded)
    prior_two = from_behind(prior_one, "z", 1)
    prior_two = jnp.where(frame_index >= 1, prior_two, padded)
    history = jnp.stack([prior_two, prior_one, padded]).reshape(3, tile_rows + 2, width, LC)
    history = jnp.pad(history, ((0, 0), (0, 0), (1, 1), (0, 0)))
    windows = [
        history[time_tap, row_tap : row_tap + tile_rows, column_tap : column_tap + width, :]
        for time_tap in range(3)
        for row_tap in range(3)
        for column_tap in range(3)
    ]
    columns = jnp.concatenate(windows, axis=-1).reshape(tile_rows * width, 27 * LC)
    summed = (
        jnp.dot(columns, decoder_kernel, preferred_element_type=jnp.float32) + decoder_bias[None, :]
    )
    return summed.astype(jnp.bfloat16).reshape(tile_rows, width, decoder_kernel.shape[1])


def solution(mesh):
    blocks = mesh.shape["blk"]
    fine = Mesh(
        mesh.devices.reshape(FRAMES, blocks // FRAMES // 2, 2, mesh.shape["head"], mesh.shape["dec"]),
        ROWS,
    )
    rows = ("z", "x", "core")
    in_specs = (
        P(rows, ("head", "dec")),
        P(rows, ("head", "dec")),
        P(rows, ("head", "dec")),
        P(),
        P(ROWS, None),
        P(("head", "dec"), None),
        P(),
        P(),
        P(),
        P(),
        P(),
        P(),
    )
    out_specs = P(ROWS, None, None)
    return jax.shard_map(
        per_device, mesh=fine, in_specs=in_specs, out_specs=out_specs, check_vma=False
    )
```

```python
import functools

import jax
import jax.numpy as jnp
from jax import lax
from jax.experimental import pallas as pl
from jax.experimental.pallas import tpu as pltpu
from jax.sharding import Mesh
from jax.sharding import PartitionSpec as P

DH = 128
LC = 16
FRAMES = 8
PW = 32

ROWS = ("z", "x", "core", "head", "dec")


def padded_2(cells, sides, width):
    for axis, dim in sides:
        count = lax.axis_size(axis)
        ends = count - 1
        head = lax.slice_in_dim(cells, 0, width, axis=dim)
        tail = lax.slice_in_dim(cells, cells.shape[dim] - width, cells.shape[dim], axis=dim)
        cells = jnp.concatenate(
            [
                lax.ppermute(tail, axis, [(i, (i + 1) % count) for i in range(ends)]),
                cells,
                lax.ppermute(head, axis, [((i + 1) % count, i) for i in range(ends)]),
            ],
            axis=dim,
        )
    return cells


def from_behind(x, axis, by):
    peers = lax.axis_size(axis)
    pairs = [(i, i + by) for i in range(peers) if 0 <= i + by < peers]
    return lax.ppermute(x, axis, pairs)


def attend_kernel(head_count, part_rows, sp_ref, q_ref, kv_ref, o_ref, m_sc, l_sc, acc_sc):
    step = pl.program_id(0)
    frame_now = sp_ref[0]
    first = sp_ref[1]
    frame = first + step
    hd = head_count * DH

    @pl.when(step == 0)
    def _():
        m_sc[...] = jnp.full(m_sc.shape, -1e30, jnp.float32)
        l_sc[...] = jnp.zeros(l_sc.shape, jnp.float32)
        acc_sc[...] = jnp.zeros(acc_sc.shape, jnp.float32)

    for h in range(head_count):
        seen = (frame <= frame_now) & (frame >= frame_now - sp_ref[2 + h])

        @pl.when(seen)
        def _():
            q = q_ref[:, h * DH:(h + 1) * DH]
            for c in range(kv_ref.shape[0]):
                k = kv_ref[c, :, h * DH:(h + 1) * DH]
                v = kv_ref[c, :, hd + h * DH:hd + (h + 1) * DH]
                s = lax.dot_general(
                    q, k, (((1,), (1,)), ((), ())), preferred_element_type=jnp.float32
                ) * DH ** (-0.5)
                m_old = m_sc[h]
                m_new = jnp.maximum(m_old, jnp.max(s, axis=1, keepdims=True))
                alpha = jnp.exp(m_old - m_new)
                p = jnp.exp(s - m_new).astype(jnp.bfloat16)
                l_sc[h] = alpha * l_sc[h] + jnp.sum(p.astype(jnp.float32), axis=1, keepdims=True)
                acc_sc[h] = alpha * acc_sc[h] + jnp.dot(p, v, preferred_element_type=jnp.float32)
                m_sc[h] = m_new

    @pl.when(step == pl.num_programs(0) - 1)
    def _():
        for h in range(head_count):
            o_ref[:, h * DH:(h + 1) * DH] = (acc_sc[h] / l_sc[h]).astype(o_ref.dtype)


def attend(scalars, queries, kv):
    parts, frames, part_rows, width = kv.shape
    rows, hd = queries.shape
    head_count = hd // DH

    def kv_map(step, sp):
        return (0, jnp.minimum(sp[1] + step, sp[0]), 0, 0)

    flops = 4 * rows * parts * part_rows * hd * 6
    return pl.pallas_call(
        functools.partial(attend_kernel, head_count, part_rows),
        out_shape=jax.ShapeDtypeStruct((rows, hd), jnp.bfloat16),
        grid_spec=pltpu.PrefetchScalarGridSpec(
            num_scalar_prefetch=1,
            grid=(frames,),
            in_specs=[
                pl.BlockSpec((rows, hd), lambda step, sp: (0, 0)),
                pl.BlockSpec((parts, None, part_rows, width), kv_map),
            ],
            out_specs=pl.BlockSpec((rows, hd), lambda step, sp: (0, 0)),
            scratch_shapes=[
                pltpu.VMEM((head_count, rows, 1), jnp.float32),
                pltpu.VMEM((head_count, rows, 1), jnp.float32),
                pltpu.VMEM((head_count, rows, DH), jnp.float32),
            ],
        ),
        compiler_params=pltpu.CompilerParams(
            dimension_semantics=("arbitrary",), vmem_limit_bytes=48 * 1024 * 1024
        ),
        cost_estimate=pl.CostEstimate(
            flops=flops,
            transcendentals=rows * parts * part_rows * head_count * 6,
            bytes_accessed=parts * part_rows * width * 2 * 6 + rows * hd * 4,
        ),
    )(scalars, queries, kv)


def per_device(
    queries,
    key_vectors,
    values,
    lookback,
    residual,
    out_weight,
    branch_gate,
    final_shift,
    final_scale,
    final_weight,
    decoder_kernel,
    decoder_bias,
):
    slab_rows = queries.shape[0]
    head_count = queries.shape[1] // DH
    frame_index = lax.axis_index("z")
    lookback_heads = lax.dynamic_slice_in_dim(
        lookback, lax.axis_index(("head", "dec")) * head_count, head_count
    )
    first_frame = jnp.maximum(frame_index - jnp.max(lookback_heads), 0)
    scalars = jnp.concatenate(
        [jnp.stack([frame_index, first_frame]).astype(jnp.int32), lookback_heads.astype(jnp.int32)]
    )

    kv = jnp.concatenate([key_vectors, values], axis=1)
    kv = lax.all_gather(kv, ("z", "x", "core"), axis=0, tiled=True)
    kv = kv.reshape(1, FRAMES, kv.shape[0] // FRAMES, kv.shape[1])
    attended = attend(scalars, queries, kv)

    tokens_dev = slab_rows // lax.axis_size(("head", "dec"))
    shares = lax.axis_size(("head", "dec"))
    partial = jnp.dot(attended, out_weight, preferred_element_type=jnp.float32).astype(jnp.bfloat16)
    partial = lax.all_to_all(
        partial.reshape(shares, tokens_dev, partial.shape[1]), ("head", "dec"), 0, 0, tiled=False
    )
    projected = jnp.sum(partial.astype(jnp.float32), axis=0)
    hidden = residual.astype(jnp.float32) + branch_gate[None, :] * projected
    center = jnp.mean(hidden, axis=1, keepdims=True)
    spread = jnp.mean((hidden - center) ** 2, axis=1, keepdims=True)
    normed = (
        (hidden - center) * lax.rsqrt(spread + 1e-06) * (1.0 + final_scale[None, :])
        + final_shift[None, :]
    ).astype(jnp.bfloat16)
    patches = jnp.dot(normed, final_weight, preferred_element_type=jnp.float32).astype(jnp.bfloat16)
    patch_rows = tokens_dev // PW
    tile_rows = 2 * patch_rows
    width = 2 * PW
    tile = (
        patches.reshape(patch_rows, PW, 2, 2, LC)
        .transpose(0, 2, 1, 3, 4)
        .reshape(tile_rows, width * LC)
    )
    per_frame = lax.axis_size(ROWS) // FRAMES
    first_row = tile[:1]
    last_row = tile[-1:]

    def window_of(back):
        shift = back * per_frame
        return jnp.concatenate(
            [
                from_behind(last_row, ROWS, shift + 1),
                tile if back == 0 else from_behind(tile, ROWS, shift),
                from_behind(first_row, ROWS, shift - 1),
            ],
            axis=0,
        )

    padded = window_of(0)
    prior_one = jnp.where(frame_index >= 1, window_of(1), padded)
    prior_two = jnp.where(frame_index >= 2, window_of(2), prior_one)
    history = jnp.stack([prior_two, prior_one, padded]).reshape(3, tile_rows + 2, width, LC)
    history = jnp.pad(history, ((0, 0), (0, 0), (1, 1), (0, 0)))
    windows = [
        history[time_tap, row_tap : row_tap + tile_rows, column_tap : column_tap + width, :]
        for time_tap in range(3)
        for row_tap in range(3)
        for column_tap in range(3)
    ]
    columns = jnp.concatenate(windows, axis=-1).reshape(tile_rows * width, 27 * LC)
    summed = (
        jnp.dot(columns, decoder_kernel, preferred_element_type=jnp.float32) + decoder_bias[None, :]
    )
    return summed.astype(jnp.bfloat16).reshape(tile_rows, width, decoder_kernel.shape[1])


def solution(mesh):
    blocks = mesh.shape["blk"]
    fine = Mesh(
        mesh.devices.reshape(FRAMES, blocks // FRAMES // 2, 2, mesh.shape["head"], mesh.shape["dec"]),
        ROWS,
    )
    rows = ("z", "x", "core")
    in_specs = (
        P(rows, ("head", "dec")),
        P(rows, ("head", "dec")),
        P(rows, ("head", "dec")),
        P(),
        P(ROWS, None),
        P(("head", "dec"), None),
        P(),
        P(),
        P(),
        P(),
        P(),
        P(),
    )
    out_specs = P(ROWS, None, None)
    return jax.shard_map(
        per_device, mesh=fine, in_specs=in_specs, out_specs=out_specs, check_vma=False
    )
```

```python
import functools

import jax
import jax.numpy as jnp
from jax import lax
from jax.experimental import pallas as pl
from jax.experimental.pallas import tpu as pltpu
from jax.sharding import Mesh
from jax.sharding import PartitionSpec as P

DH = 128
LC = 16
FRAMES = 8
PW = 32

ROWS = ("z", "x", "core", "head", "dec")


def from_behind(x, axis, by):
    peers = lax.axis_size(axis)
    pairs = [(i, i + by) for i in range(peers) if 0 <= i + by < peers]
    return lax.ppermute(x, axis, pairs)


def attend_kernel(head_count, part_rows, sp_ref, q_ref, kv_ref, o_ref, m_sc, l_sc, acc_sc):
    step = pl.program_id(0)
    frame_now = sp_ref[0]
    first = sp_ref[1]
    frame = first + step
    hd = head_count * DH

    @pl.when(step == 0)
    def _():
        m_sc[...] = jnp.full(m_sc.shape, -1e30, jnp.float32)
        l_sc[...] = jnp.zeros(l_sc.shape, jnp.float32)
        acc_sc[...] = jnp.zeros(acc_sc.shape, jnp.float32)

    to_log2 = DH ** (-0.5) * 1.4426950408889634
    ones = jnp.ones((kv_ref.shape[1], DH), jnp.bfloat16)
    for h in range(head_count):
        seen = (frame <= frame_now) & (frame >= frame_now - sp_ref[2 + h])

        @pl.when(seen)
        def _():
            q = q_ref[:, h * DH:(h + 1) * DH]
            for c in range(kv_ref.shape[0]):
                k = kv_ref[c, :, h * DH:(h + 1) * DH]
                v = kv_ref[c, :, hd + h * DH:hd + (h + 1) * DH]
                s = lax.dot_general(
                    q, k, (((1,), (1,)), ((), ())), preferred_element_type=jnp.float32
                ) * to_log2
                m_old = m_sc[h]
                m_new = jnp.maximum(m_old, jnp.max(s, axis=1, keepdims=True))
                alpha = jnp.exp2(m_old - m_new)
                p = jnp.exp2(s - m_new).astype(jnp.bfloat16)
                total = jnp.dot(p, ones, preferred_element_type=jnp.float32)[:, :1]
                l_sc[h] = alpha * l_sc[h] + total
                acc_sc[h] = alpha * acc_sc[h] + jnp.dot(p, v, preferred_element_type=jnp.float32)
                m_sc[h] = m_new

    @pl.when(step == pl.num_programs(0) - 1)
    def _():
        for h in range(head_count):
            o_ref[:, h * DH:(h + 1) * DH] = (acc_sc[h] / l_sc[h]).astype(o_ref.dtype)


def attend(scalars, queries, kv):
    parts, frames, part_rows, width = kv.shape
    rows, hd = queries.shape
    head_count = hd // DH

    def kv_map(step, sp):
        return (0, jnp.minimum(sp[1] + step, sp[0]), 0, 0)

    flops = 4 * rows * parts * part_rows * hd * 6
    return pl.pallas_call(
        functools.partial(attend_kernel, head_count, part_rows),
        out_shape=jax.ShapeDtypeStruct((rows, hd), jnp.bfloat16),
        grid_spec=pltpu.PrefetchScalarGridSpec(
            num_scalar_prefetch=1,
            grid=(frames,),
            in_specs=[
                pl.BlockSpec((rows, hd), lambda step, sp: (0, 0)),
                pl.BlockSpec((parts, None, part_rows, width), kv_map),
            ],
            out_specs=pl.BlockSpec((rows, hd), lambda step, sp: (0, 0)),
            scratch_shapes=[
                pltpu.VMEM((head_count, rows, 1), jnp.float32),
                pltpu.VMEM((head_count, rows, 1), jnp.float32),
                pltpu.VMEM((head_count, rows, DH), jnp.float32),
            ],
        ),
        compiler_params=pltpu.CompilerParams(
            dimension_semantics=("arbitrary",), vmem_limit_bytes=48 * 1024 * 1024
        ),
        cost_estimate=pl.CostEstimate(
            flops=flops,
            transcendentals=rows * parts * part_rows * head_count * 6,
            bytes_accessed=parts * part_rows * width * 2 * 6 + rows * hd * 4,
        ),
    )(scalars, queries, kv)


def per_device(
    queries,
    key_vectors,
    values,
    lookback,
    residual,
    out_weight,
    branch_gate,
    final_shift,
    final_scale,
    final_weight,
    decoder_kernel,
    decoder_bias,
):
    slab_rows = queries.shape[0]
    head_count = queries.shape[1] // DH
    frame_index = lax.axis_index("z")
    lookback_heads = lax.dynamic_slice_in_dim(
        lookback, lax.axis_index(("head", "dec")) * head_count, head_count
    )
    first_frame = jnp.maximum(frame_index - jnp.max(lookback_heads), 0)
    scalars = jnp.concatenate(
        [jnp.stack([frame_index, first_frame]).astype(jnp.int32), lookback_heads.astype(jnp.int32)]
    )

    kv = jnp.concatenate([key_vectors, values], axis=1)
    kv = lax.all_gather(kv, ("z", "x", "core"), axis=0, tiled=True)
    kv = kv.reshape(1, FRAMES, kv.shape[0] // FRAMES, kv.shape[1])
    attended = attend(scalars, queries, kv)

    tokens_dev = slab_rows // lax.axis_size(("head", "dec"))
    shares = lax.axis_size(("head", "dec"))
    weight_all = lax.all_to_all(
        jnp.broadcast_to(out_weight[None], (shares,) + out_weight.shape),
        ("head", "dec"), 0, 0, tiled=False,
    ).reshape(shares * out_weight.shape[0], out_weight.shape[1])
    mine = lax.all_to_all(
        attended.reshape(shares, tokens_dev, attended.shape[1]), ("head", "dec"), 0, 0, tiled=False
    )
    mine = mine.transpose(1, 0, 2).reshape(tokens_dev, shares * attended.shape[1])
    projected = jnp.dot(mine, weight_all, preferred_element_type=jnp.float32)
    hidden = residual.astype(jnp.float32) + branch_gate[None, :] * projected
    center = jnp.mean(hidden, axis=1, keepdims=True)
    spread = jnp.mean((hidden - center) ** 2, axis=1, keepdims=True)
    normed = (
        (hidden - center) * lax.rsqrt(spread + 1e-06) * (1.0 + final_scale[None, :])
        + final_shift[None, :]
    ).astype(jnp.bfloat16)
    patches = jnp.dot(normed, final_weight, preferred_element_type=jnp.float32).astype(jnp.bfloat16)
    patch_rows = tokens_dev // PW
    tile_rows = 2 * patch_rows
    width = 2 * PW
    tile = (
        patches.reshape(patch_rows, PW, 2, 2, LC)
        .transpose(0, 2, 1, 3, 4)
        .reshape(tile_rows, width * LC)
    )
    per_frame = lax.axis_size(ROWS) // FRAMES
    first_row = tile[:1]
    last_row = tile[-1:]

    padded = jnp.concatenate(
        [from_behind(last_row, ROWS, 1), tile, from_behind(first_row, ROWS, -1)], axis=0
    )
    prior_one = jnp.where(frame_index >= 1, from_behind(padded, ROWS, per_frame), padded)
    prior_two = jnp.where(frame_index >= 2, from_behind(padded, ROWS, 2 * per_frame), prior_one)
    history = jnp.stack([prior_two, prior_one, padded]).reshape(3, tile_rows + 2, width, LC)
    history = jnp.pad(history, ((0, 0), (0, 0), (1, 1), (0, 0)))
    windows = [
        history[time_tap, row_tap : row_tap + tile_rows, column_tap : column_tap + width, :]
        for time_tap in range(3)
        for row_tap in range(3)
        for column_tap in range(3)
    ]
    columns = jnp.concatenate(windows, axis=-1).reshape(tile_rows * width, 27 * LC)
    summed = (
        jnp.dot(columns, decoder_kernel, preferred_element_type=jnp.float32) + decoder_bias[None, :]
    )
    return summed.astype(jnp.bfloat16).reshape(tile_rows, width, decoder_kernel.shape[1])


def solution(mesh):
    blocks = mesh.shape["blk"]
    fine = Mesh(
        mesh.devices.reshape(FRAMES, blocks // FRAMES // 2, 2, mesh.shape["head"], mesh.shape["dec"]),
        ROWS,
    )
    rows = ("z", "x", "core")
    in_specs = (
        P(rows, ("head", "dec")),
        P(rows, ("head", "dec")),
        P(rows, ("head", "dec")),
        P(),
        P(ROWS, None),
        P(("head", "dec"), None),
        P(),
        P(),
        P(),
        P(),
        P(),
        P(),
    )
    out_specs = P(ROWS, None, None)
    return jax.shard_map(
        per_device, mesh=fine, in_specs=in_specs, out_specs=out_specs, check_vma=False
    )
```

```python
import functools

import jax
import jax.numpy as jnp
from jax import lax
from jax.experimental import pallas as pl
from jax.experimental.pallas import tpu as pltpu
from jax.sharding import Mesh
from jax.sharding import PartitionSpec as P

DH = 128
LC = 16
FRAMES = 8
PW = 32

ROWS = ("z", "x", "core", "head", "dec")


def from_behind(x, axis, by):
    peers = lax.axis_size(axis)
    pairs = [(i, i + by) for i in range(peers) if 0 <= i + by < peers]
    return lax.ppermute(x, axis, pairs)


def attend_kernel(head_count, sp_ref, q_ref, kv_ref, o_ref, m_sc, l_sc, acc_sc):
    step = pl.program_id(0)
    frame_now = sp_ref[0]
    first = sp_ref[1]
    frame = first + step
    hd = head_count * DH

    @pl.when(step == 0)
    def _():
        m_sc[...] = jnp.full(m_sc.shape, -1e30, jnp.float32)
        l_sc[...] = jnp.zeros(l_sc.shape, jnp.float32)
        acc_sc[...] = jnp.zeros(acc_sc.shape, jnp.float32)

    to_log2 = DH ** (-0.5) * 1.4426950408889634
    for h in range(head_count):
        seen = (frame <= frame_now) & (frame >= frame_now - sp_ref[2 + h])

        @pl.when(seen)
        def _():
            q = q_ref[:, h * DH:(h + 1) * DH]
            for c in range(kv_ref.shape[0]):
                k = kv_ref[c, :, h * DH:(h + 1) * DH]
                v = kv_ref[c, :, hd + h * DH:hd + (h + 1) * DH]
                st = lax.dot_general(
                    k, q, (((1,), (1,)), ((), ())), preferred_element_type=jnp.float32
                ) * to_log2
                m_old = m_sc[h]
                m_new = jnp.maximum(m_old, jnp.max(st, axis=0, keepdims=True))
                alpha = jnp.exp2(m_old - m_new)
                pt = jnp.exp2(st - m_new).astype(jnp.bfloat16)
                l_sc[h] = alpha * l_sc[h] + jnp.sum(pt.astype(jnp.float32), axis=0, keepdims=True)
                acc_sc[h] = alpha * acc_sc[h] + lax.dot_general(
                    v, pt, (((0,), (0,)), ((), ())), preferred_element_type=jnp.float32
                )
                m_sc[h] = m_new

    @pl.when(step == pl.num_programs(0) - 1)
    def _():
        for h in range(head_count):
            o_ref[:, h * DH:(h + 1) * DH] = (acc_sc[h] / l_sc[h]).T.astype(o_ref.dtype)


def attend(scalars, queries, kv):
    parts, frames, part_rows, width = kv.shape
    rows, hd = queries.shape
    head_count = hd // DH

    def kv_map(step, sp):
        return (0, jnp.minimum(sp[1] + step, sp[0]), 0, 0)

    flops = 4 * rows * parts * part_rows * hd * 6
    return pl.pallas_call(
        functools.partial(attend_kernel, head_count),
        out_shape=jax.ShapeDtypeStruct((rows, hd), jnp.bfloat16),
        grid_spec=pltpu.PrefetchScalarGridSpec(
            num_scalar_prefetch=1,
            grid=(frames,),
            in_specs=[
                pl.BlockSpec((rows, hd), lambda step, sp: (0, 0)),
                pl.BlockSpec((parts, None, part_rows, width), kv_map),
            ],
            out_specs=pl.BlockSpec((rows, hd), lambda step, sp: (0, 0)),
            scratch_shapes=[
                pltpu.VMEM((head_count, 1, rows), jnp.float32),
                pltpu.VMEM((head_count, 1, rows), jnp.float32),
                pltpu.VMEM((head_count, DH, rows), jnp.float32),
            ],
        ),
        compiler_params=pltpu.CompilerParams(
            dimension_semantics=("arbitrary",), vmem_limit_bytes=48 * 1024 * 1024
        ),
        cost_estimate=pl.CostEstimate(
            flops=flops,
            transcendentals=rows * parts * part_rows * head_count * 6,
            bytes_accessed=parts * part_rows * width * 2 * 6 + rows * hd * 4,
        ),
    )(scalars, queries, kv)


def per_device(
    queries,
    key_vectors,
    values,
    lookback,
    residual,
    out_weight,
    branch_gate,
    final_shift,
    final_scale,
    final_weight,
    decoder_kernel,
    decoder_bias,
):
    slab_rows = queries.shape[0]
    head_count = queries.shape[1] // DH
    frame_index = lax.axis_index("z")
    lookback_heads = lax.dynamic_slice_in_dim(
        lookback, lax.axis_index(("head", "dec")) * head_count, head_count
    )
    first_frame = jnp.maximum(frame_index - jnp.max(lookback_heads), 0)
    scalars = jnp.concatenate(
        [jnp.stack([frame_index, first_frame]).astype(jnp.int32), lookback_heads.astype(jnp.int32)]
    )

    kv = jnp.concatenate([key_vectors, values], axis=1)
    kv = lax.all_gather(kv, ("z", "x", "core"), axis=0, tiled=True)
    kv = kv.reshape(1, FRAMES, kv.shape[0] // FRAMES, kv.shape[1])
    attended = attend(scalars, queries, kv)

    tokens_dev = slab_rows // lax.axis_size(("head", "dec"))
    shares = lax.axis_size(("head", "dec"))
    weight_all = lax.all_to_all(
        jnp.broadcast_to(out_weight[None], (shares,) + out_weight.shape),
        ("head", "dec"), 0, 0, tiled=False,
    ).reshape(shares * out_weight.shape[0], out_weight.shape[1])
    mine = lax.all_to_all(
        attended.reshape(shares, tokens_dev, attended.shape[1]), ("head", "dec"), 0, 0, tiled=False
    )
    mine = mine.transpose(1, 0, 2).reshape(tokens_dev, shares * attended.shape[1])
    projected = lax.dot_general(
        weight_all, mine, (((0,), (1,)), ((), ())), preferred_element_type=jnp.float32
    ).T
    hidden = residual.astype(jnp.float32) + branch_gate[None, :] * projected
    center = jnp.mean(hidden, axis=1, keepdims=True)
    spread = jnp.mean((hidden - center) ** 2, axis=1, keepdims=True)
    normed = (
        (hidden - center) * lax.rsqrt(spread + 1e-06) * (1.0 + final_scale[None, :])
        + final_shift[None, :]
    ).astype(jnp.bfloat16)
    patches = jnp.dot(normed, final_weight, preferred_element_type=jnp.float32).astype(jnp.bfloat16)
    patch_rows = tokens_dev // PW
    tile_rows = 2 * patch_rows
    width = 2 * PW
    tile = (
        patches.reshape(patch_rows, PW, 2, 2, LC)
        .transpose(0, 2, 1, 3, 4)
        .reshape(tile_rows, width * LC)
    )
    per_frame = lax.axis_size(ROWS) // FRAMES
    first_row = tile[:1]
    last_row = tile[-1:]

    padded = jnp.concatenate(
        [from_behind(last_row, ROWS, 1), tile, from_behind(first_row, ROWS, -1)], axis=0
    )
    prior_one = jnp.where(frame_index >= 1, from_behind(padded, ROWS, per_frame), padded)
    prior_two = jnp.where(frame_index >= 2, from_behind(padded, ROWS, 2 * per_frame), prior_one)
    history = jnp.stack([prior_two, prior_one, padded]).reshape(3, tile_rows + 2, width, LC)
    history = jnp.pad(history, ((0, 0), (0, 0), (1, 1), (0, 0)))
    windows = [
        history[time_tap, row_tap : row_tap + tile_rows, column_tap : column_tap + width, :]
        for time_tap in range(3)
        for row_tap in range(3)
        for column_tap in range(3)
    ]
    columns = jnp.concatenate(windows, axis=-1).reshape(tile_rows * width, 27 * LC)
    summed = (
        jnp.dot(columns, decoder_kernel, preferred_element_type=jnp.float32) + decoder_bias[None, :]
    )
    return summed.astype(jnp.bfloat16).reshape(tile_rows, width, decoder_kernel.shape[1])


def solution(mesh):
    blocks = mesh.shape["blk"]
    fine = Mesh(
        mesh.devices.reshape(FRAMES, blocks // FRAMES // 2, 2, mesh.shape["head"], mesh.shape["dec"]),
        ROWS,
    )
    rows = ("z", "x", "core")
    in_specs = (
        P(rows, ("head", "dec")),
        P(rows, ("head", "dec")),
        P(rows, ("head", "dec")),
        P(),
        P(ROWS, None),
        P(("head", "dec"), None),
        P(),
        P(),
        P(),
        P(),
        P(),
        P(),
    )
    out_specs = P(ROWS, None, None)
    return jax.shard_map(
        per_device, mesh=fine, in_specs=in_specs, out_specs=out_specs, check_vma=False
    )
```

```python
import functools

import jax
import jax.numpy as jnp
from jax import lax
from jax.experimental import pallas as pl
from jax.experimental.pallas import tpu as pltpu
from jax.sharding import Mesh
from jax.sharding import PartitionSpec as P

DH = 128
LC = 16
FRAMES = 8
PW = 32

ROWS = ("z", "x", "core", "head", "dec")


def from_behind(x, axis, by):
    peers = lax.axis_size(axis)
    pairs = [(i, i + by) for i in range(peers) if 0 <= i + by < peers]
    return lax.ppermute(x, axis, pairs)


def attend_kernel(head_count, sp_ref, q_ref, kv_ref, o_ref, m_sc, l_sc, acc_sc):
    step = pl.program_id(0)
    frame_now = sp_ref[0]
    first = sp_ref[1]
    frame = first + step
    hd = head_count * DH

    @pl.when(step == 0)
    def _():
        m_sc[...] = jnp.full(m_sc.shape, -1e30, jnp.float32)
        l_sc[...] = jnp.zeros(l_sc.shape, jnp.float32)
        acc_sc[...] = jnp.zeros(acc_sc.shape, jnp.float32)

    to_log2 = DH ** (-0.5) * 1.4426950408889634
    for h in range(head_count):
        seen = (frame <= frame_now) & (frame >= frame_now - sp_ref[2 + h])

        @pl.when(seen)
        def _():
            q = q_ref[:, h * DH:(h + 1) * DH]
            for c in range(kv_ref.shape[0]):
                k = kv_ref[c, :, h * DH:(h + 1) * DH]
                v = kv_ref[c, :, hd + h * DH:hd + (h + 1) * DH]
                st = lax.dot_general(
                    k, q, (((1,), (1,)), ((), ())), preferred_element_type=jnp.float32
                ) * to_log2
                m_old = m_sc[h]
                m_new = jnp.maximum(m_old, jnp.max(st, axis=0, keepdims=True))
                alpha = jnp.exp2(m_old - m_new)
                pt = jnp.exp2(st - m_new).astype(jnp.bfloat16)
                l_sc[h] = alpha * l_sc[h] + jnp.sum(pt.astype(jnp.float32), axis=0, keepdims=True)
                acc_sc[h] = alpha * acc_sc[h] + lax.dot_general(
                    v, pt, (((0,), (0,)), ((), ())), preferred_element_type=jnp.float32
                )
                m_sc[h] = m_new

    @pl.when(step == pl.num_programs(0) - 1)
    def _():
        for h in range(head_count):
            o_ref[:, h * DH:(h + 1) * DH] = (acc_sc[h] / l_sc[h]).T.astype(o_ref.dtype)


def attend(scalars, queries, kv):
    parts, frames, part_rows, width = kv.shape
    rows, hd = queries.shape
    head_count = hd // DH

    def kv_map(step, sp):
        return (0, jnp.minimum(sp[1] + step, sp[0]), 0, 0)

    flops = 4 * rows * parts * part_rows * hd * 6
    return pl.pallas_call(
        functools.partial(attend_kernel, head_count),
        out_shape=jax.ShapeDtypeStruct((rows, hd), jnp.bfloat16),
        grid_spec=pltpu.PrefetchScalarGridSpec(
            num_scalar_prefetch=1,
            grid=(frames,),
            in_specs=[
                pl.BlockSpec((rows, hd), lambda step, sp: (0, 0)),
                pl.BlockSpec((parts, None, part_rows, width), kv_map),
            ],
            out_specs=pl.BlockSpec((rows, hd), lambda step, sp: (0, 0)),
            scratch_shapes=[
                pltpu.VMEM((head_count, 1, rows), jnp.float32),
                pltpu.VMEM((head_count, 1, rows), jnp.float32),
                pltpu.VMEM((head_count, DH, rows), jnp.float32),
            ],
        ),
        compiler_params=pltpu.CompilerParams(
            dimension_semantics=("arbitrary",), vmem_limit_bytes=48 * 1024 * 1024
        ),
        cost_estimate=pl.CostEstimate(
            flops=flops,
            transcendentals=rows * parts * part_rows * head_count * 6,
            bytes_accessed=parts * part_rows * width * 2 * 6 + rows * hd * 4,
        ),
    )(scalars, queries, kv)


def project_kernel(w_ref, m_ref, o_ref):
    @pl.when(pl.program_id(1) == 0)
    def _():
        o_ref[...] = jnp.zeros(o_ref.shape, jnp.float32)

    o_ref[...] += jnp.dot(w_ref[...], m_ref[...], preferred_element_type=jnp.float32)


def project(weight_t, mine_t):
    parts, out_dim, in_dim = weight_t.shape
    tokens = mine_t.shape[2]
    block = 512
    return pl.pallas_call(
        project_kernel,
        out_shape=jax.ShapeDtypeStruct((out_dim, tokens), jnp.float32),
        grid=(out_dim // block, parts),
        in_specs=[
            pl.BlockSpec((None, block, in_dim), lambda i, j: (j, i, 0)),
            pl.BlockSpec((None, in_dim, tokens), lambda i, j: (j, 0, 0)),
        ],
        out_specs=pl.BlockSpec((block, tokens), lambda i, j: (i, 0)),
        compiler_params=pltpu.CompilerParams(dimension_semantics=("arbitrary", "arbitrary")),
        cost_estimate=pl.CostEstimate(
            flops=2 * parts * out_dim * in_dim * tokens,
            transcendentals=0,
            bytes_accessed=parts * (out_dim * in_dim * 2 + in_dim * tokens * 2) + out_dim * tokens * 4,
        ),
    )(weight_t, mine_t)


def per_device(
    queries,
    key_vectors,
    values,
    lookback,
    residual,
    out_weight,
    branch_gate,
    final_shift,
    final_scale,
    final_weight,
    decoder_kernel,
    decoder_bias,
):
    slab_rows = queries.shape[0]
    head_count = queries.shape[1] // DH
    frame_index = lax.axis_index("z")
    lookback_heads = lax.dynamic_slice_in_dim(
        lookback, lax.axis_index(("head", "dec")) * head_count, head_count
    )
    first_frame = jnp.maximum(frame_index - jnp.max(lookback_heads), 0)
    scalars = jnp.concatenate(
        [jnp.stack([frame_index, first_frame]).astype(jnp.int32), lookback_heads.astype(jnp.int32)]
    )

    kv = jnp.concatenate([key_vectors, values], axis=1)
    kv = lax.all_gather(kv, ("z", "x", "core"), axis=0, tiled=True)
    kv = kv.reshape(1, FRAMES, kv.shape[0] // FRAMES, kv.shape[1])
    shares = lax.axis_size(("head", "dec"))
    weight_t = out_weight.T
    weight_all = lax.all_to_all(
        jnp.broadcast_to(weight_t[None], (shares,) + weight_t.shape), ("head", "dec"), 0, 0, tiled=False
    )
    kv, weight_all = lax.optimization_barrier((kv, weight_all))
    attended = attend(scalars, queries, kv)

    tokens_dev = slab_rows // lax.axis_size(("head", "dec"))
    shares = lax.axis_size(("head", "dec"))
    mine = lax.all_to_all(
        attended.reshape(shares, tokens_dev, attended.shape[1]), ("head", "dec"), 0, 0, tiled=False
    )
    mine_t = mine.transpose(0, 2, 1)
    projected = project(weight_all, mine_t).T
    hidden = residual.astype(jnp.float32) + branch_gate[None, :] * projected
    center = jnp.mean(hidden, axis=1, keepdims=True)
    spread = jnp.mean((hidden - center) ** 2, axis=1, keepdims=True)
    normed = (
        (hidden - center) * lax.rsqrt(spread + 1e-06) * (1.0 + final_scale[None, :])
        + final_shift[None, :]
    ).astype(jnp.bfloat16)
    patches = jnp.dot(normed, final_weight, preferred_element_type=jnp.float32).astype(jnp.bfloat16)
    patch_rows = tokens_dev // PW
    tile_rows = 2 * patch_rows
    width = 2 * PW
    tile = (
        patches.reshape(patch_rows, PW, 2, 2, LC)
        .transpose(0, 2, 1, 3, 4)
        .reshape(tile_rows, width * LC)
    )
    per_frame = lax.axis_size(ROWS) // FRAMES
    first_row = tile[:1]
    last_row = tile[-1:]

    padded = jnp.concatenate(
        [from_behind(last_row, ROWS, 1), tile, from_behind(first_row, ROWS, -1)], axis=0
    )
    prior_one = jnp.where(frame_index >= 1, from_behind(padded, ROWS, per_frame), padded)
    prior_two = jnp.where(frame_index >= 2, from_behind(padded, ROWS, 2 * per_frame), prior_one)
    history = jnp.stack([prior_two, prior_one, padded]).reshape(3, tile_rows + 2, width, LC)
    history = jnp.pad(history, ((0, 0), (0, 0), (1, 1), (0, 0)))
    windows = [
        history[time_tap, row_tap : row_tap + tile_rows, column_tap : column_tap + width, :]
        for time_tap in range(3)
        for row_tap in range(3)
        for column_tap in range(3)
    ]
    columns = jnp.concatenate(windows, axis=-1).reshape(tile_rows * width, 27 * LC)
    summed = (
        jnp.dot(columns, decoder_kernel, preferred_element_type=jnp.float32) + decoder_bias[None, :]
    )
    return summed.astype(jnp.bfloat16).reshape(tile_rows, width, decoder_kernel.shape[1])


def solution(mesh):
    blocks = mesh.shape["blk"]
    fine = Mesh(
        mesh.devices.reshape(FRAMES, blocks // FRAMES // 2, 2, mesh.shape["head"], mesh.shape["dec"]),
        ROWS,
    )
    rows = ("z", "x", "core")
    in_specs = (
        P(rows, ("head", "dec")),
        P(rows, ("head", "dec")),
        P(rows, ("head", "dec")),
        P(),
        P(ROWS, None),
        P(("head", "dec"), None),
        P(),
        P(),
        P(),
        P(),
        P(),
        P(),
    )
    out_specs = P(ROWS, None, None)
    return jax.shard_map(
        per_device, mesh=fine, in_specs=in_specs, out_specs=out_specs, check_vma=False
    )
```

```python
import functools

import jax
import jax.numpy as jnp
from jax import lax
from jax.experimental import pallas as pl
from jax.experimental.pallas import tpu as pltpu
from jax.sharding import Mesh
from jax.sharding import PartitionSpec as P

DH = 128
LC = 16
FRAMES = 8
PW = 32
WINDOW = 5

ROWS = ("z", "x", "core", "head", "dec")


def from_behind(x, axis, by):
    peers = lax.axis_size(axis)
    pairs = [(i, i + by) for i in range(peers) if 0 <= i + by < peers]
    return lax.ppermute(x, axis, pairs)


def attend_kernel(head_count, sp_ref, q_ref, kv_ref, o_ref, m_sc, l_sc, acc_sc):
    step = pl.program_id(0)
    frame_now = sp_ref[0]
    first = sp_ref[1]
    frame = first + step
    hd = head_count * DH

    @pl.when(step == 0)
    def _():
        m_sc[...] = jnp.full(m_sc.shape, -1e30, jnp.float32)
        l_sc[...] = jnp.zeros(l_sc.shape, jnp.float32)
        acc_sc[...] = jnp.zeros(acc_sc.shape, jnp.float32)

    to_log2 = DH ** (-0.5) * 1.4426950408889634
    for h in range(head_count):
        seen = (frame <= frame_now) & (frame >= frame_now - sp_ref[2 + h])

        @pl.when(seen)
        def _():
            q = q_ref[:, h * DH:(h + 1) * DH]
            for c in range(kv_ref.shape[0]):
                k = kv_ref[c, :, h * DH:(h + 1) * DH]
                v = kv_ref[c, :, hd + h * DH:hd + (h + 1) * DH]
                st = lax.dot_general(
                    k, q, (((1,), (1,)), ((), ())), preferred_element_type=jnp.float32
                ) * to_log2
                m_old = m_sc[h]
                m_new = jnp.maximum(m_old, jnp.max(st, axis=0, keepdims=True))
                alpha = jnp.exp2(m_old - m_new)
                pt = jnp.exp2(st - m_new).astype(jnp.bfloat16)
                l_sc[h] = alpha * l_sc[h] + jnp.sum(pt.astype(jnp.float32), axis=0, keepdims=True)
                acc_sc[h] = alpha * acc_sc[h] + lax.dot_general(
                    v, pt, (((0,), (0,)), ((), ())), preferred_element_type=jnp.float32
                )
                m_sc[h] = m_new

    @pl.when(step == pl.num_programs(0) - 1)
    def _():
        for h in range(head_count):
            o_ref[:, h * DH:(h + 1) * DH] = (acc_sc[h] / l_sc[h]).T.astype(o_ref.dtype)


def attend(scalars, queries, kv):
    parts, frames, part_rows, width = kv.shape
    rows, hd = queries.shape
    head_count = hd // DH

    def kv_map(step, sp):
        return (0, jnp.minimum(sp[1] + step, sp[0]), 0, 0)

    flops = 4 * rows * parts * part_rows * hd * 6
    return pl.pallas_call(
        functools.partial(attend_kernel, head_count),
        out_shape=jax.ShapeDtypeStruct((rows, hd), jnp.bfloat16),
        grid_spec=pltpu.PrefetchScalarGridSpec(
            num_scalar_prefetch=1,
            grid=(min(frames, WINDOW + 1),),
            in_specs=[
                pl.BlockSpec((rows, hd), lambda step, sp: (0, 0)),
                pl.BlockSpec((parts, None, part_rows, width), kv_map),
            ],
            out_specs=pl.BlockSpec((rows, hd), lambda step, sp: (0, 0)),
            scratch_shapes=[
                pltpu.VMEM((head_count, 1, rows), jnp.float32),
                pltpu.VMEM((head_count, 1, rows), jnp.float32),
                pltpu.VMEM((head_count, DH, rows), jnp.float32),
            ],
        ),
        compiler_params=pltpu.CompilerParams(
            dimension_semantics=("arbitrary",), vmem_limit_bytes=48 * 1024 * 1024
        ),
        cost_estimate=pl.CostEstimate(
            flops=flops,
            transcendentals=rows * parts * part_rows * head_count * 6,
            bytes_accessed=parts * part_rows * width * 2 * 6 + rows * hd * 4,
        ),
    )(scalars, queries, kv)


def per_device(
    queries,
    key_vectors,
    values,
    lookback,
    residual,
    out_weight,
    branch_gate,
    final_shift,
    final_scale,
    final_weight,
    decoder_kernel,
    decoder_bias,
):
    slab_rows = queries.shape[0]
    head_count = queries.shape[1] // DH
    frame_index = lax.axis_index("z")
    lookback_heads = lax.dynamic_slice_in_dim(
        lookback, lax.axis_index(("head", "dec")) * head_count, head_count
    )
    first_frame = jnp.maximum(frame_index - jnp.max(lookback_heads), 0)
    scalars = jnp.concatenate(
        [jnp.stack([frame_index, first_frame]).astype(jnp.int32), lookback_heads.astype(jnp.int32)]
    )

    kv = jnp.concatenate([key_vectors, values], axis=1)
    kv = lax.all_gather(kv, ("z", "x", "core"), axis=0, tiled=True)
    kv = kv.reshape(1, FRAMES, kv.shape[0] // FRAMES, kv.shape[1])
    attended = attend(scalars, queries, kv)

    tokens_dev = slab_rows // lax.axis_size(("head", "dec"))
    shares = lax.axis_size(("head", "dec"))
    weight_all = lax.all_to_all(
        jnp.broadcast_to(out_weight[None], (shares,) + out_weight.shape),
        ("head", "dec"), 0, 0, tiled=False,
    ).reshape(shares * out_weight.shape[0], out_weight.shape[1])
    mine = lax.all_to_all(
        attended.reshape(shares, tokens_dev, attended.shape[1]), ("head", "dec"), 0, 0, tiled=False
    )
    mine = mine.transpose(1, 0, 2).reshape(tokens_dev, shares * attended.shape[1])
    projected = lax.dot_general(
        weight_all, mine, (((0,), (1,)), ((), ())), preferred_element_type=jnp.float32
    ).T
    hidden = residual.astype(jnp.float32) + branch_gate[None, :] * projected
    center = jnp.mean(hidden, axis=1, keepdims=True)
    spread = jnp.mean((hidden - center) ** 2, axis=1, keepdims=True)
    normed = (
        (hidden - center) * lax.rsqrt(spread + 1e-06) * (1.0 + final_scale[None, :])
        + final_shift[None, :]
    ).astype(jnp.bfloat16)
    patches = jnp.dot(normed, final_weight, preferred_element_type=jnp.float32).astype(jnp.bfloat16)
    patch_rows = tokens_dev // PW
    tile_rows = 2 * patch_rows
    width = 2 * PW
    tile = (
        patches.reshape(patch_rows, PW, 2, 2, LC)
        .transpose(0, 2, 1, 3, 4)
        .reshape(tile_rows, width * LC)
    )
    per_frame = lax.axis_size(ROWS) // FRAMES
    first_row = tile[:1]
    last_row = tile[-1:]

    padded = jnp.concatenate(
        [from_behind(last_row, ROWS, 1), tile, from_behind(first_row, ROWS, -1)], axis=0
    )
    prior_one = jnp.where(frame_index >= 1, from_behind(padded, ROWS, per_frame), padded)
    prior_two = jnp.where(frame_index >= 2, from_behind(padded, ROWS, 2 * per_frame), prior_one)
    history = jnp.stack([prior_two, prior_one, padded]).reshape(3, tile_rows + 2, width, LC)
    history = jnp.pad(history, ((0, 0), (0, 0), (1, 1), (0, 0)))
    windows = [
        history[time_tap, row_tap : row_tap + tile_rows, column_tap : column_tap + width, :]
        for time_tap in range(3)
        for row_tap in range(3)
        for column_tap in range(3)
    ]
    columns = jnp.concatenate(windows, axis=-1).reshape(tile_rows * width, 27 * LC)
    summed = (
        jnp.dot(columns, decoder_kernel, preferred_element_type=jnp.float32) + decoder_bias[None, :]
    )
    return summed.astype(jnp.bfloat16).reshape(tile_rows, width, decoder_kernel.shape[1])


def solution(mesh):
    blocks = mesh.shape["blk"]
    fine = Mesh(
        mesh.devices.reshape(FRAMES, blocks // FRAMES // 2, 2, mesh.shape["head"], mesh.shape["dec"]),
        ROWS,
    )
    rows = ("z", "x", "core")
    in_specs = (
        P(rows, ("head", "dec")),
        P(rows, ("head", "dec")),
        P(rows, ("head", "dec")),
        P(),
        P(ROWS, None),
        P(("head", "dec"), None),
        P(),
        P(),
        P(),
        P(),
        P(),
        P(),
    )
    out_specs = P(ROWS, None, None)
    return jax.shard_map(
        per_device, mesh=fine, in_specs=in_specs, out_specs=out_specs, check_vma=False
    )
```

```python
import functools

import jax
import jax.numpy as jnp
from jax import lax
from jax.experimental import pallas as pl
from jax.experimental.pallas import tpu as pltpu
from jax.sharding import Mesh
from jax.sharding import PartitionSpec as P

DH = 128
LC = 16
FRAMES = 8
PW = 32

ROWS = ("z", "x", "core", "head", "dec")


def from_behind(x, axis, by):
    peers = lax.axis_size(axis)
    pairs = [(i, i + by) for i in range(peers) if 0 <= i + by < peers]
    return lax.ppermute(x, axis, pairs)


def attend_kernel(head_count, sp_ref, q_ref, kv_ref, o_ref, m_sc, l_sc, acc_sc):
    step = pl.program_id(0)
    frame_now = sp_ref[0]
    first = sp_ref[1]
    frame = first + step
    hd = head_count * DH

    @pl.when(step == 0)
    def _():
        m_sc[...] = jnp.full(m_sc.shape, -1e30, jnp.float32)
        l_sc[...] = jnp.zeros(l_sc.shape, jnp.float32)
        acc_sc[...] = jnp.zeros(acc_sc.shape, jnp.float32)

    to_log2 = DH ** (-0.5) * 1.4426950408889634
    for h in range(head_count):
        seen = (frame <= frame_now) & (frame >= frame_now - sp_ref[2 + h])

        @pl.when(seen)
        def _():
            q = q_ref[:, h * DH:(h + 1) * DH]
            for c in range(1):
                k = kv_ref[0, :, h * DH:(h + 1) * DH]
                v = kv_ref[1, :, h * DH:(h + 1) * DH]
                st = lax.dot_general(
                    k, q, (((1,), (1,)), ((), ())), preferred_element_type=jnp.float32
                ) * to_log2
                m_old = m_sc[h]
                m_new = jnp.maximum(m_old, jnp.max(st, axis=0, keepdims=True))
                alpha = jnp.exp2(m_old - m_new)
                pt = jnp.exp2(st - m_new).astype(jnp.bfloat16)
                l_sc[h] = alpha * l_sc[h] + jnp.sum(pt.astype(jnp.float32), axis=0, keepdims=True)
                acc_sc[h] = alpha * acc_sc[h] + lax.dot_general(
                    v, pt, (((0,), (0,)), ((), ())), preferred_element_type=jnp.float32
                )
                m_sc[h] = m_new

    @pl.when(step == pl.num_programs(0) - 1)
    def _():
        for h in range(head_count):
            o_ref[:, h * DH:(h + 1) * DH] = (acc_sc[h] / l_sc[h]).T.astype(o_ref.dtype)


def attend(scalars, queries, kv):
    parts, frames, part_rows, width = kv.shape
    rows, hd = queries.shape
    head_count = hd // DH

    def kv_map(step, sp):
        return (0, jnp.minimum(sp[1] + step, sp[0]), 0, 0)

    flops = 4 * rows * part_rows * hd * 6
    return pl.pallas_call(
        functools.partial(attend_kernel, head_count),
        out_shape=jax.ShapeDtypeStruct((rows, hd), jnp.bfloat16),
        grid_spec=pltpu.PrefetchScalarGridSpec(
            num_scalar_prefetch=1,
            grid=(frames,),
            in_specs=[
                pl.BlockSpec((rows, hd), lambda step, sp: (0, 0)),
                pl.BlockSpec((parts, None, part_rows, width), kv_map),
            ],
            out_specs=pl.BlockSpec((rows, hd), lambda step, sp: (0, 0)),
            scratch_shapes=[
                pltpu.VMEM((head_count, 1, rows), jnp.float32),
                pltpu.VMEM((head_count, 1, rows), jnp.float32),
                pltpu.VMEM((head_count, DH, rows), jnp.float32),
            ],
        ),
        compiler_params=pltpu.CompilerParams(
            dimension_semantics=("arbitrary",), vmem_limit_bytes=48 * 1024 * 1024
        ),
        cost_estimate=pl.CostEstimate(
            flops=flops,
            transcendentals=rows * part_rows * head_count * 6,
            bytes_accessed=parts * part_rows * width * 2 * 6 + rows * hd * 4,
        ),
    )(scalars, queries, kv)


def per_device(
    queries,
    key_vectors,
    values,
    lookback,
    residual,
    out_weight,
    branch_gate,
    final_shift,
    final_scale,
    final_weight,
    decoder_kernel,
    decoder_bias,
):
    slab_rows = queries.shape[0]
    head_count = queries.shape[1] // DH
    frame_index = lax.axis_index("z")
    lookback_heads = lax.dynamic_slice_in_dim(
        lookback, lax.axis_index(("head", "dec")) * head_count, head_count
    )
    first_frame = jnp.maximum(frame_index - jnp.max(lookback_heads), 0)
    scalars = jnp.concatenate(
        [jnp.stack([frame_index, first_frame]).astype(jnp.int32), lookback_heads.astype(jnp.int32)]
    )

    kv = jnp.stack([key_vectors, values])
    kv = lax.all_gather(kv, ("z", "x", "core"), axis=1, tiled=True)
    kv = kv.reshape(2, FRAMES, kv.shape[1] // FRAMES, kv.shape[2])
    attended = attend(scalars, queries, kv)

    tokens_dev = slab_rows // lax.axis_size(("head", "dec"))
    shares = lax.axis_size(("head", "dec"))
    weight_all = lax.all_to_all(
        jnp.broadcast_to(out_weight[None], (shares,) + out_weight.shape),
        ("head", "dec"), 0, 0, tiled=False,
    ).reshape(shares * out_weight.shape[0], out_weight.shape[1])
    mine = lax.all_to_all(
        attended.reshape(shares, tokens_dev, attended.shape[1]), ("head", "dec"), 0, 0, tiled=False
    )
    mine = mine.transpose(1, 0, 2).reshape(tokens_dev, shares * attended.shape[1])
    projected = lax.dot_general(
        weight_all, mine, (((0,), (1,)), ((), ())), preferred_element_type=jnp.float32
    ).T
    hidden = residual.astype(jnp.float32) + branch_gate[None, :] * projected
    center = jnp.mean(hidden, axis=1, keepdims=True)
    spread = jnp.mean((hidden - center) ** 2, axis=1, keepdims=True)
    normed = (
        (hidden - center) * lax.rsqrt(spread + 1e-06) * (1.0 + final_scale[None, :])
        + final_shift[None, :]
    ).astype(jnp.bfloat16)
    patches = jnp.dot(normed, final_weight, preferred_element_type=jnp.float32).astype(jnp.bfloat16)
    patch_rows = tokens_dev // PW
    tile_rows = 2 * patch_rows
    width = 2 * PW
    tile = (
        patches.reshape(patch_rows, PW, 2, 2, LC)
        .transpose(0, 2, 1, 3, 4)
        .reshape(tile_rows, width * LC)
    )
    per_frame = lax.axis_size(ROWS) // FRAMES
    first_row = tile[:1]
    last_row = tile[-1:]

    padded = jnp.concatenate(
        [from_behind(last_row, ROWS, 1), tile, from_behind(first_row, ROWS, -1)], axis=0
    )
    prior_one = jnp.where(frame_index >= 1, from_behind(padded, ROWS, per_frame), padded)
    prior_two = jnp.where(frame_index >= 2, from_behind(padded, ROWS, 2 * per_frame), prior_one)
    history = jnp.stack([prior_two, prior_one, padded]).reshape(3, tile_rows + 2, width, LC)
    history = jnp.pad(history, ((0, 0), (0, 0), (1, 1), (0, 0)))
    windows = [
        history[time_tap, row_tap : row_tap + tile_rows, column_tap : column_tap + width, :]
        for time_tap in range(3)
        for row_tap in range(3)
        for column_tap in range(3)
    ]
    columns = jnp.concatenate(windows, axis=-1).reshape(tile_rows * width, 27 * LC)
    summed = (
        jnp.dot(columns, decoder_kernel, preferred_element_type=jnp.float32) + decoder_bias[None, :]
    )
    return summed.astype(jnp.bfloat16).reshape(tile_rows, width, decoder_kernel.shape[1])


def solution(mesh):
    blocks = mesh.shape["blk"]
    fine = Mesh(
        mesh.devices.reshape(FRAMES, blocks // FRAMES // 2, 2, mesh.shape["head"], mesh.shape["dec"]),
        ROWS,
    )
    rows = ("z", "x", "core")
    in_specs = (
        P(rows, ("head", "dec")),
        P(rows, ("head", "dec")),
        P(rows, ("head", "dec")),
        P(),
        P(ROWS, None),
        P(("head", "dec"), None),
        P(),
        P(),
        P(),
        P(),
        P(),
        P(),
    )
    out_specs = P(ROWS, None, None)
    return jax.shard_map(
        per_device, mesh=fine, in_specs=in_specs, out_specs=out_specs, check_vma=False
    )
```
